512 devices in a mesh: row: 16 (over z), col: 32 (over x, y, core).
Axes of the slice: x: 4, y: 4, z: 16, core: 2. Of those that a mesh axis runs over, the one named last changes fastest.
Arguments:
- feats: bfloat16 [8192, 4096], P('row', 'col'), may hold values from -6 to 6
- prior_factor: bfloat16 [8192, 2048], P('row', 'col'), may hold values from -0.02 to 0.02, as said below
- ridge: float32 [1024], P('col'), may hold values from 0.5 to 2
Outputs:
- factor: float32 [8192, 1024], P('row', 'col')
The draws below stay inside these ranges and needn't reach their ends.
Inputs may be any that keep to these rules, and one draw needn't show every extreme that they name: `prior_factor`: entries are independent.
All inputs are finite; a program needn't handle non-finite values.
Results may differ from the reference program's by a relative error of at most 0.0003.
Values may be sent and summed in bfloat16 or wider, within the bound.
No kernel may reach another device: no remote copies, remote signals or barrier semaphores. Data moves between devices by JAX's collectives and lax.ppermute only.
A program may use at most 128 MiB of HBM per device.

```python
import math
import jax
import jax.numpy as jnp
from jax import lax

EDGES = 4096
PRIOR = 2048
PANEL = 512
KCOLS = 1024
ROWS_DEV = 512
NROWS = 8192
N_ROW = 16


def draw_prior_factor(key, part):
    shape = (NROWS, PRIOR)
    values = jnp.clip(jax.random.normal(key, shape, jnp.float32) * 0.008, -0.0198, 0.0198)
    return values.astype(jnp.bfloat16)


def steps_of(key, extent, shards, low, top_value):
    def one(dim, blocks):
        heights = jax.random.uniform(jax.random.fold_in(jax.random.fold_in(key, 6), dim), (blocks,), jnp.float32, low / len(shards), top_value / len(shards))
        return jnp.repeat(jnp.exp(heights), extent[dim] // blocks).reshape((-1,) + (1,) * (len(extent) - dim - 1))

    loudness = one(*shards[0])
    for cut in shards[1:]:
        loudness = loudness * one(*cut)
    return loudness


def normal_values(stream_key, dims, spread, limit, shards=(), dtype=jnp.bfloat16):
    result = spread * jax.random.normal(stream_key, dims, jnp.float32)
    if shards:
        result = result * steps_of(stream_key, dims, shards, -0.22, 0.18)
    return jnp.clip(result, -limit, limit).astype(dtype)


def setup_inputs(seed: int = 0) -> dict:
    splits = jax.random.split(jax.random.key(seed), 4)
    return {
        "feats": normal_values(splits[0], (NROWS, EDGES), 1.0, 6.0, ((0, 16), (1, 32))),
        "prior_factor": draw_prior_factor(jax.random.fold_in(splits[3], 71), 0),
        "ridge": jnp.clip(jnp.exp(math.log(2.0) - 1.3862944 * jax.random.uniform(splits[2], (KCOLS,), jnp.float32) ** steps_of(splits[2], (KCOLS,), ((0, 32),), -0.2, 0.2)), 0.5, 2.0),
    }


def subject_rows(parts, groups, count):
    width = parts.shape[-1]
    return parts.reshape(groups, count, width).transpose(1, 0, 2).reshape(groups * count, width)

def panel_cholesky(block, panel):
    top = jnp.linalg.cholesky(block[:panel, :panel])
    lower_left = jax.scipy.linalg.solve_triangular(top, block[panel:, :panel].T, lower=True).T
    rest = block[panel:, panel:] - jnp.dot(lower_left, lower_left.T, precision=lax.Precision.HIGHEST)
    bottom = jnp.linalg.cholesky(rest)
    upper = jnp.concatenate([top, jnp.zeros((panel, block.shape[0] - panel), jnp.float32)], axis=1)
    lower = jnp.concatenate([lower_left, bottom], axis=1)
    return jnp.concatenate([upper, lower], axis=0)

def reference(feats, prior_factor, ridge):
    subj_feats = subject_rows(feats, N_ROW, ROWS_DEV)
    subj_prior = subject_rows(prior_factor, N_ROW, ROWS_DEV)
    gram = jnp.dot(subj_feats.astype(jnp.float32), subj_feats[:KCOLS].T.astype(jnp.float32), preferred_element_type=jnp.float32)
    update = jnp.dot(subj_prior.astype(jnp.float32), subj_prior[:KCOLS].T.astype(jnp.float32), preferred_element_type=jnp.float32)
    wide = subj_feats.astype(jnp.float32)
    squares = jnp.sum(wide * wide, axis=1)
    kernel = jnp.exp(-(squares[:, None] + squares[None, :KCOLS] - 2.0 * gram) / EDGES)
    subject = lax.broadcasted_iota(jnp.int32, (NROWS, KCOLS), 0)
    column = lax.broadcasted_iota(jnp.int32, (NROWS, KCOLS), 1)
    system = kernel + jnp.where(subject == column, ridge[None, :], jnp.zeros_like(kernel)) - update
    diag_factor = panel_cholesky(system[:KCOLS], PANEL)
    solved = jax.scipy.linalg.solve_triangular(diag_factor, system.T, lower=True).T
    return solved.reshape(ROWS_DEV, N_ROW, KCOLS).transpose(1, 0, 2).reshape(NROWS, KCOLS)
```

```python
import jax
import jax.numpy as jnp
from jax import lax
from jax.experimental import pallas as pl
from jax.experimental.pallas import tpu as pltpu
from jax.sharding import PartitionSpec as P

EDGES = 4096
PANEL = 512
BLK = 128
SUB = 8
HI = lax.Precision.HIGHEST
TN = (((0,), (0,)), ((), ()))


def _chol_rows_kernel(a_ref, o_ref):
    n, width = a_ref.shape[0], a_ref.shape[1]
    o_ref[...] = a_ref[...]
    nb = n // BLK
    for k in range(nb):
        r0 = k * BLK
        m = width - r0

        def sub_panel(p, carry, r0=r0, m=m):
            base = pl.multiple_of(p * SUB, SUB)
            rows = o_ref[pl.ds(r0 + base, SUB), pl.ds(r0, m)]
            lane = lax.broadcasted_iota(jnp.int32, (SUB, m), 1)
            sub = lax.broadcasted_iota(jnp.int32, (SUB, m), 0)
            lane_d = lax.broadcasted_iota(jnp.int32, (SUB, BLK), 1)
            sub_d = lax.broadcasted_iota(jnp.int32, (SUB, BLK), 0)
            pick = lane_d == base + sub_d
            sub_c = lax.broadcasted_iota(jnp.int32, (SUB, 1), 0)
            for t in range(SUB):
                rowt = jnp.broadcast_to(rows[t:t + 1, :], (SUB, m))
                c = jnp.sum(jnp.where(pick, rowt[:, :BLK], 0.0), axis=1, keepdims=True)
                piv = jnp.sum(jnp.where(sub_c == t, c, 0.0), axis=0, keepdims=True)
                inv = 1.0 / jnp.sqrt(piv)
                u = jnp.where(lane >= base + t, rowt * inv, 0.0)
                rows = jnp.where(sub > t, rows - (c * (inv * inv)) * rowt,
                                 jnp.where(sub == t, u, rows))
            o_ref[pl.ds(r0 + base, SUB), pl.ds(r0, m)] = rows
            upd = lax.dot_general(rows[:, :BLK], rows, TN, precision=HI,
                                  preferred_element_type=jnp.float32)
            blk = o_ref[pl.ds(r0, BLK), pl.ds(r0, m)]
            below = lax.broadcasted_iota(jnp.int32, (BLK, m), 0) >= base + SUB
            o_ref[pl.ds(r0, BLK), pl.ds(r0, m)] = jnp.where(below, blk - upd, blk)
            return carry

        lax.fori_loop(0, BLK // SUB, sub_panel, 0)
        for j in range(k + 1, nb):
            c0 = j * BLK
            coef = o_ref[pl.ds(r0, BLK), pl.ds(c0, BLK)]
            right = o_ref[pl.ds(r0, BLK), pl.ds(c0, width - c0)]
            upd = lax.dot_general(coef, right, TN, precision=HI,
                                  preferred_element_type=jnp.float32)
            o_ref[pl.ds(c0, BLK), pl.ds(c0, width - c0)] -= upd


def chol_rows(aug, interpret=False):
    return pl.pallas_call(
        _chol_rows_kernel,
        out_shape=jax.ShapeDtypeStruct(aug.shape, jnp.float32),
        compiler_params=pltpu.CompilerParams(vmem_limit_bytes=48 * 1024 * 1024),
        interpret=interpret,
    )(aug)


def in_one_piece(arrays, axis, dim, along):
    widths = [a.shape[along] for a in arrays]
    both = jnp.concatenate(arrays, axis=along)
    whole = lax.all_gather(both, axis, axis=dim, tiled=True)
    return tuple(jnp.split(whole, [sum(widths[:k]) for k in range(1, len(widths))], axis=along))


def copy_for_each(x, axis):
    count = lax.axis_size(axis)
    return lax.all_to_all(jnp.broadcast_to(x[None], (count, *x.shape)), axis, 0, 0, tiled=True)


def of_everyone(x, axis):
    return copy_for_each(x, axis).sum(axis=0)


def together(arrays, axis):
    ends = [0]
    for a in arrays:
        ends.append(ends[-1] + a.size)
    subtotal = of_everyone(jnp.concatenate([a.ravel() for a in arrays]), axis)
    return tuple((subtotal[b:e].reshape(a.shape) for a, b, e in zip(arrays, ends, ends[1:])))


def in_one_piece_2(arrays, axis, dim, along):
    both = jnp.concatenate(arrays, axis=along)
    whole, at, gathered = (lax.psum_scatter(both, axis, scatter_dimension=dim, tiled=True), 0, [])
    for a in arrays:
        gathered.append(lax.slice_in_dim(whole, at, at + a.shape[along], axis=along))
        at += a.shape[along]
    return tuple(gathered)


def joined_along(tiles, dim):
    dims = list(tiles.shape[1:])
    dims[dim] *= tiles.shape[0]
    return jnp.moveaxis(tiles, 0, dim).reshape(dims)


def gather_directly(x, axis, dim):
    tiles = copy_for_each(x, axis)
    return joined_along(tiles, dim)


def subject_rows(parts, groups, count):
    width = parts.shape[-1]
    return parts.reshape(groups, count, width).transpose(1, 0, 2).reshape(groups * count, width)


def body(feats, prior_factor, ridge):
    groups = lax.axis_size("row")
    lanes = lax.axis_size("col")
    row_pos = lax.axis_index("row")
    col_pos = lax.axis_index("col")
    rows_here = feats.shape[0]
    cols_here = ridge.shape[0]
    total_cols = cols_here * lanes
    leading = total_cols // groups
    col_feats, col_prior = in_one_piece((feats[:leading], prior_factor[:leading]), "row", 0, 1)
    col_feats = subject_rows(col_feats, groups, leading)
    col_prior = subject_rows(col_prior, groups, leading)
    gram_part = jnp.dot(feats, col_feats.T, preferred_element_type=jnp.float32)
    update_part = jnp.dot(prior_factor, col_prior.T, preferred_element_type=jnp.float32)
    wide_feats = feats.astype(jnp.float32)
    wide_cols = col_feats.astype(jnp.float32)
    row_sq, col_sq = together(
        (jnp.sum(wide_feats * wide_feats, axis=1), jnp.sum(wide_cols * wide_cols, axis=1)), "col"
    )
    gram, update = in_one_piece_2((gram_part, update_part), "col", 1, 0)
    col_start = col_pos * cols_here
    own_sq = lax.dynamic_slice_in_dim(col_sq, col_start, cols_here)
    kernel = jnp.exp(-(row_sq[:, None] + own_sq[None, :] - 2.0 * gram) / EDGES)
    subject = lax.broadcasted_iota(jnp.int32, (rows_here, cols_here), 0) * groups + row_pos
    column = lax.broadcasted_iota(jnp.int32, (rows_here, cols_here), 1) + col_start
    system = kernel + jnp.where(subject == column, ridge[None, :], jnp.zeros_like(kernel)) - update
    head = system[:leading]
    by_rows = gather_directly(head, "row", 0)
    by_cols = lax.all_gather(by_rows, "col", axis=1, tiled=True)
    square = subject_rows(by_cols, groups, leading)
    wide_rows = gather_directly(system, "col", 1)
    n = square.shape[0]
    i = lax.broadcasted_iota(jnp.int32, (n, n), 0)
    j = lax.broadcasted_iota(jnp.int32, (n, n), 1)
    flipped = square.T
    same = (i < PANEL) == (j < PANEL)
    sym = jnp.where(same, (square + flipped) * 0.5, jnp.where(i < j, flipped, square))
    done = chol_rows(jnp.concatenate([sym, wide_rows.T], axis=1))
    solved_t = lax.dynamic_slice_in_dim(done[:, n:], col_start, cols_here, 0)
    return solved_t.T


def solution(mesh):
    return jax.shard_map(
        body,
        mesh=mesh,
        in_specs=(P("row", "col"), P("row", "col"), P("col")),
        out_specs=P("row", "col"),
        check_vma=False,
    )
```

```python
import jax
import jax.numpy as jnp
from jax import lax
from jax.experimental import pallas as pl
from jax.experimental.pallas import tpu as pltpu
from jax.sharding import PartitionSpec as P

EDGES = 4096
PANEL = 512
BLK = 128
SUB = 8
HI = lax.Precision.HIGHEST
TN = (((0,), (0,)), ((), ()))


def _diag(d_ref):
    wide = 2 * BLK
    lane = lax.broadcasted_iota(jnp.int32, (SUB, wide), 1)
    sub = lax.broadcasted_iota(jnp.int32, (SUB, wide), 0)
    lane_d = lax.broadcasted_iota(jnp.int32, (SUB, BLK), 1)
    sub_d = lax.broadcasted_iota(jnp.int32, (SUB, BLK), 0)
    rows = d_ref[0:SUB, :]
    for p in range(BLK // SUB):
        base = p * SUB
        pick = lane_d == base + sub_d
        for t in range(SUB):
            rowt = jnp.broadcast_to(rows[t:t + 1, :], (SUB, wide))
            head = rowt[:, :BLK]
            c = jnp.sum(jnp.where(pick, head, 0.0), axis=1, keepdims=True)
            piv = jnp.sum(jnp.where(lane_d == base + t, head, 0.0), axis=1, keepdims=True)
            inv = lax.rsqrt(piv)
            u = jnp.where(lane >= base + t, rowt * inv, 0.0)
            rows = jnp.where(sub > t, rows - (c * (inv * inv)) * rowt,
                             jnp.where(sub == t, u, rows))
        d_ref[base:base + SUB, :] = rows
        nb0 = base + SUB
        if nb0 < BLK:
            nxt = d_ref[nb0:nb0 + SUB, :]
            pick2 = lane_d == nb0 + sub_d
            for t in range(SUB):
                rowt = jnp.broadcast_to(rows[t:t + 1, :], (SUB, wide))
                coef = jnp.sum(jnp.where(pick2, rowt[:, :BLK], 0.0), axis=1, keepdims=True)
                nxt = nxt - coef * rowt
            lo = nb0 + SUB
            if lo < BLK:
                upd = lax.dot_general(rows[:, :BLK], rows, TN, precision=HI,
                                      preferred_element_type=jnp.float32)
                d_ref[lo:BLK, :] = d_ref[lo:BLK, :] - upd[lo:, :]
            rows = nxt


def _chol_rows_kernel(a_ref, o_ref, d_ref):
    n, width = a_ref.shape[0], a_ref.shape[1]
    o_ref[...] = a_ref[...]
    nb = n // BLK
    wide = 2 * BLK
    eye = (lax.broadcasted_iota(jnp.int32, (BLK, BLK), 0)
           == lax.broadcasted_iota(jnp.int32, (BLK, BLK), 1)).astype(jnp.float32)
    for k in range(nb):
        r0 = k * BLK
        m = width - r0
        d_ref[:, :BLK] = o_ref[pl.ds(r0, BLK), pl.ds(r0, BLK)]
        d_ref[:, BLK:] = eye

        _diag(d_ref)
        o_ref[pl.ds(r0, BLK), pl.ds(r0, BLK)] = d_ref[:, :BLK]
        if m > BLK:
            rest = o_ref[pl.ds(r0, BLK), pl.ds(r0 + BLK, m - BLK)]
            o_ref[pl.ds(r0, BLK), pl.ds(r0 + BLK, m - BLK)] = jnp.dot(
                d_ref[:, BLK:], rest, precision=HI, preferred_element_type=jnp.float32)
        for j in range(k + 1, nb):
            c0 = j * BLK
            coef = o_ref[pl.ds(r0, BLK), pl.ds(c0, BLK)]
            right = o_ref[pl.ds(r0, BLK), pl.ds(c0, width - c0)]
            upd = lax.dot_general(coef, right, TN, precision=HI,
                                  preferred_element_type=jnp.float32)
            o_ref[pl.ds(c0, BLK), pl.ds(c0, width - c0)] -= upd


def chol_rows(aug, interpret=False):
    return pl.pallas_call(
        _chol_rows_kernel,
        out_shape=jax.ShapeDtypeStruct(aug.shape, jnp.float32),
        scratch_shapes=[pltpu.VMEM((BLK, 2 * BLK), jnp.float32)],
        compiler_params=pltpu.CompilerParams(vmem_limit_bytes=48 * 1024 * 1024),
        interpret=interpret,
    )(aug)


def in_one_piece(arrays, axis, dim, along):
    widths = [a.shape[along] for a in arrays]
    both = jnp.concatenate(arrays, axis=along)
    whole = lax.all_gather(both, axis, axis=dim, tiled=True)
    return tuple(jnp.split(whole, [sum(widths[:k]) for k in range(1, len(widths))], axis=along))


def copy_for_each(x, axis):
    count = lax.axis_size(axis)
    return lax.all_to_all(jnp.broadcast_to(x[None], (count, *x.shape)), axis, 0, 0, tiled=True)


def of_everyone(x, axis):
    return copy_for_each(x, axis).sum(axis=0)


def together(arrays, axis):
    ends = [0]
    for a in arrays:
        ends.append(ends[-1] + a.size)
    subtotal = of_everyone(jnp.concatenate([a.ravel() for a in arrays]), axis)
    return tuple((subtotal[b:e].reshape(a.shape) for a, b, e in zip(arrays, ends, ends[1:])))


def in_one_piece_2(arrays, axis, dim, along):
    both = jnp.concatenate(arrays, axis=along)
    whole, at, gathered = (lax.psum_scatter(both, axis, scatter_dimension=dim, tiled=True), 0, [])
    for a in arrays:
        gathered.append(lax.slice_in_dim(whole, at, at + a.shape[along], axis=along))
        at += a.shape[along]
    return tuple(gathered)


def joined_along(tiles, dim):
    dims = list(tiles.shape[1:])
    dims[dim] *= tiles.shape[0]
    return jnp.moveaxis(tiles, 0, dim).reshape(dims)


def gather_directly(x, axis, dim):
    tiles = copy_for_each(x, axis)
    return joined_along(tiles, dim)


def subject_rows(parts, groups, count):
    width = parts.shape[-1]
    return parts.reshape(groups, count, width).transpose(1, 0, 2).reshape(groups * count, width)


def body(feats, prior_factor, ridge):
    groups = lax.axis_size("row")
    lanes = lax.axis_size("col")
    row_pos = lax.axis_index("row")
    col_pos = lax.axis_index("col")
    rows_here = feats.shape[0]
    cols_here = ridge.shape[0]
    total_cols = cols_here * lanes
    leading = total_cols // groups
    col_feats, col_prior = in_one_piece((feats[:leading], prior_factor[:leading]), "row", 0, 1)
    col_feats = subject_rows(col_feats, groups, leading)
    col_prior = subject_rows(col_prior, groups, leading)
    gram_part = jnp.dot(feats, col_feats.T, preferred_element_type=jnp.float32)
    update_part = jnp.dot(prior_factor, col_prior.T, preferred_element_type=jnp.float32)
    wide_feats = feats.astype(jnp.float32)
    wide_cols = col_feats.astype(jnp.float32)
    row_sq, col_sq = together(
        (jnp.sum(wide_feats * wide_feats, axis=1), jnp.sum(wide_cols * wide_cols, axis=1)), "col"
    )
    gram, update = in_one_piece_2((gram_part, update_part), "col", 1, 0)
    col_start = col_pos * cols_here
    own_sq = lax.dynamic_slice_in_dim(col_sq, col_start, cols_here)
    kernel = jnp.exp(-(row_sq[:, None] + own_sq[None, :] - 2.0 * gram) / EDGES)
    subject = lax.broadcasted_iota(jnp.int32, (rows_here, cols_here), 0) * groups + row_pos
    column = lax.broadcasted_iota(jnp.int32, (rows_here, cols_here), 1) + col_start
    system = kernel + jnp.where(subject == column, ridge[None, :], jnp.zeros_like(kernel)) - update
    head = system[:leading]
    by_rows = gather_directly(head, "row", 0)
    by_cols = lax.all_gather(by_rows, "col", axis=1, tiled=True)
    square = subject_rows(by_cols, groups, leading)
    wide_rows = gather_directly(system, "col", 1)
    n = square.shape[0]
    i = lax.broadcasted_iota(jnp.int32, (n, n), 0)
    j = lax.broadcasted_iota(jnp.int32, (n, n), 1)
    flipped = square.T
    same = (i < PANEL) == (j < PANEL)
    sym = jnp.where(same, (square + flipped) * 0.5, jnp.where(i < j, flipped, square))
    done = chol_rows(jnp.concatenate([sym, wide_rows.T], axis=1))
    solved_t = lax.dynamic_slice_in_dim(done[:, n:], col_start, cols_here, 0)
    return solved_t.T


def solution(mesh):
    return jax.shard_map(
        body,
        mesh=mesh,
        in_specs=(P("row", "col"), P("row", "col"), P("col")),
        out_specs=P("row", "col"),
        check_vma=False,
    )
```

```python
import jax
import jax.numpy as jnp
from jax import lax
from jax.experimental import pallas as pl
from jax.experimental.pallas import tpu as pltpu
from jax.sharding import PartitionSpec as P

EDGES = 4096
PANEL = 512
BLK = 128
SUB = 8
HI = lax.Precision.HIGHEST
TN = (((0,), (0,)), ((), ()))


def _diag(d_ref):
    wide = 2 * BLK
    lane = lax.broadcasted_iota(jnp.int32, (SUB, wide), 1)
    sub = lax.broadcasted_iota(jnp.int32, (SUB, wide), 0)
    lane_d = lax.broadcasted_iota(jnp.int32, (SUB, BLK), 1)
    sub_d = lax.broadcasted_iota(jnp.int32, (SUB, BLK), 0)
    rows = d_ref[0:SUB, :]
    for p in range(BLK // SUB):
        base = p * SUB
        pick = lane_d == base + sub_d
        for t in range(SUB):
            rowt = jnp.broadcast_to(rows[t:t + 1, :], (SUB, wide))
            head = rowt[:, :BLK]
            c = jnp.sum(jnp.where(pick, head, 0.0), axis=1, keepdims=True)
            piv = jnp.sum(jnp.where(lane_d == base + t, head, 0.0), axis=1, keepdims=True)
            inv = lax.rsqrt(piv)
            u = jnp.where(lane >= base + t, rowt * inv, 0.0)
            rows = jnp.where(sub > t, rows - (c * (inv * inv)) * rowt,
                             jnp.where(sub == t, u, rows))
        d_ref[base:base + SUB, :] = rows
        nb0 = base + SUB
        if nb0 < BLK:
            nxt = d_ref[nb0:nb0 + SUB, :]
            pick2 = lane_d == nb0 + sub_d
            for t in range(SUB):
                rowt = jnp.broadcast_to(rows[t:t + 1, :], (SUB, wide))
                coef = jnp.sum(jnp.where(pick2, rowt[:, :BLK], 0.0), axis=1, keepdims=True)
                nxt = nxt - coef * rowt
            lo = nb0 + SUB
            if lo < BLK:
                upd = lax.dot_general(rows[:, :BLK], rows, TN, precision=HI,
                                      preferred_element_type=jnp.float32)
                d_ref[lo:BLK, :] = d_ref[lo:BLK, :] - upd[lo:, :]
            rows = nxt


def _chol_rows_kernel(a_ref, o_ref, d_ref):
    n, width = a_ref.shape[0], a_ref.shape[1]
    o_ref[...] = a_ref[...]
    nb = n // BLK
    wide = 2 * BLK
    eye = (lax.broadcasted_iota(jnp.int32, (BLK, BLK), 0)
           == lax.broadcasted_iota(jnp.int32, (BLK, BLK), 1)).astype(jnp.float32)
    for k in range(nb):
        r0 = k * BLK
        m = width - r0
        d_ref[:, :BLK] = o_ref[pl.ds(r0, BLK), pl.ds(r0, BLK)]
        d_ref[:, BLK:] = eye

        _diag(d_ref)
        o_ref[pl.ds(r0, BLK), pl.ds(r0, BLK)] = d_ref[:, :BLK]
        if m > BLK:
            rest = o_ref[pl.ds(r0, BLK), pl.ds(r0 + BLK, m - BLK)]
            o_ref[pl.ds(r0, BLK), pl.ds(r0 + BLK, m - BLK)] = jnp.dot(
                d_ref[:, BLK:], rest, precision=HI, preferred_element_type=jnp.float32)
        for j in range(k + 1, nb):
            c0 = j * BLK
            coef = o_ref[pl.ds(r0, BLK), pl.ds(c0, BLK)]
            right = o_ref[pl.ds(r0, BLK), pl.ds(c0, width - c0)]
            upd = lax.dot_general(coef, right, TN, precision=HI,
                                  preferred_element_type=jnp.float32)
            o_ref[pl.ds(c0, BLK), pl.ds(c0, width - c0)] -= upd


def chol_rows(aug, interpret=False):
    return pl.pallas_call(
        _chol_rows_kernel,
        out_shape=jax.ShapeDtypeStruct(aug.shape, jnp.float32),
        scratch_shapes=[pltpu.VMEM((BLK, 2 * BLK), jnp.float32)],
        compiler_params=pltpu.CompilerParams(vmem_limit_bytes=48 * 1024 * 1024),
        interpret=interpret,
    )(aug)


def in_one_piece(arrays, axis, dim, along):
    widths = [a.shape[along] for a in arrays]
    both = jnp.concatenate(arrays, axis=along)
    whole = lax.all_gather(both, axis, axis=dim, tiled=True)
    return tuple(jnp.split(whole, [sum(widths[:k]) for k in range(1, len(widths))], axis=along))


def copy_for_each(x, axis):
    count = lax.axis_size(axis)
    return lax.all_to_all(jnp.broadcast_to(x[None], (count, *x.shape)), axis, 0, 0, tiled=True)


def of_everyone(x, axis):
    return copy_for_each(x, axis).sum(axis=0)


def together(arrays, axis):
    ends = [0]
    for a in arrays:
        ends.append(ends[-1] + a.size)
    subtotal = of_everyone(jnp.concatenate([a.ravel() for a in arrays]), axis)
    return tuple((subtotal[b:e].reshape(a.shape) for a, b, e in zip(arrays, ends, ends[1:])))


def in_one_piece_2(arrays, axis, dim, along):
    both = jnp.concatenate(arrays, axis=along)
    whole, at, gathered = (lax.psum_scatter(both, axis, scatter_dimension=dim, tiled=True), 0, [])
    for a in arrays:
        gathered.append(lax.slice_in_dim(whole, at, at + a.shape[along], axis=along))
        at += a.shape[along]
    return tuple(gathered)


def joined_along(tiles, dim):
    dims = list(tiles.shape[1:])
    dims[dim] *= tiles.shape[0]
    return jnp.moveaxis(tiles, 0, dim).reshape(dims)


def gather_directly(x, axis, dim):
    tiles = copy_for_each(x, axis)
    return joined_along(tiles, dim)


def subject_rows(parts, groups, count):
    width = parts.shape[-1]
    return parts.reshape(groups, count, width).transpose(1, 0, 2).reshape(groups * count, width)


def body(feats, prior_factor, ridge):
    groups = lax.axis_size("row")
    lanes = lax.axis_size("col")
    row_pos = lax.axis_index("row")
    col_pos = lax.axis_index("col")
    rows_here = feats.shape[0]
    cols_here = ridge.shape[0]
    total_cols = cols_here * lanes
    leading = total_cols // groups
    col_feats, col_prior = in_one_piece((feats[:leading], prior_factor[:leading]), "row", 0, 1)
    col_feats = subject_rows(col_feats, groups, leading)
    col_prior = subject_rows(col_prior, groups, leading)
    gram_part = jnp.dot(feats, col_feats.T, preferred_element_type=jnp.float32)
    update_part = jnp.dot(prior_factor, col_prior.T, preferred_element_type=jnp.float32)
    wide_feats = feats.astype(jnp.float32)
    wide_cols = col_feats.astype(jnp.float32)
    col_start = col_pos * cols_here
    ridge_pad = lax.dynamic_update_slice_in_dim(
        jnp.zeros((total_cols,), jnp.float32), ridge, col_start, 0)
    row_sq, col_sq, ridge_all = together(
        (jnp.sum(wide_feats * wide_feats, axis=1), jnp.sum(wide_cols * wide_cols, axis=1),
         ridge_pad), "col"
    )

    def system_of(gram, update, sq, first):
        count, width = gram.shape
        start = col_start if width == cols_here else 0
        col_part = lax.dynamic_slice_in_dim(col_sq, start, width)
        kernel = jnp.exp(-(sq[:, None] + col_part[None, :] - 2.0 * gram) / EDGES)
        subject = (lax.broadcasted_iota(jnp.int32, (count, width), 0) + first) * groups + row_pos
        column = lax.broadcasted_iota(jnp.int32, (count, width), 1) + start
        ridge_part = ridge if width == cols_here else ridge_all
        diag = jnp.where(subject == column, ridge_part[None, :], jnp.zeros_like(kernel))
        return kernel + diag - update

    head_gram, head_update = in_one_piece_2(
        (gram_part[:leading], update_part[:leading]), "col", 1, 0)
    head = system_of(head_gram, head_update, row_sq[:leading], 0)
    by_rows = subject_rows(gather_directly(head, "row", 0), groups, leading)
    square = lax.all_gather(by_rows, "col", axis=1, tiled=True)
    gram_part, update_part, square = lax.optimization_barrier((gram_part, update_part, square))
    n = square.shape[0]
    i = lax.broadcasted_iota(jnp.int32, (n, n), 0)
    j = lax.broadcasted_iota(jnp.int32, (n, n), 1)
    flipped = square.T
    same = (i < PANEL) == (j < PANEL)
    sym = jnp.where(same, (square + flipped) * 0.5, jnp.where(i < j, flipped, square))
    eye = (i == j).astype(jnp.float32)
    done = chol_rows(jnp.concatenate([sym, eye], axis=1))
    inv_t = lax.dynamic_slice_in_dim(done[:, n:], col_start, cols_here, 0)

    both = lax.psum(jnp.concatenate([gram_part, update_part], axis=0), "col")
    gram, update = both[:rows_here], both[rows_here:]
    system = system_of(gram, update, row_sq, 0)
    return lax.dot_general(system, inv_t, (((1,), (1,)), ((), ())), precision=HI,
                           preferred_element_type=jnp.float32)


def solution(mesh):
    return jax.shard_map(
        body,
        mesh=mesh,
        in_specs=(P("row", "col"), P("row", "col"), P("col")),
        out_specs=P("row", "col"),
        check_vma=False,
    )
```

```python
import jax
import jax.numpy as jnp
from jax import lax
from jax.experimental import pallas as pl
from jax.experimental.pallas import tpu as pltpu
from jax.sharding import PartitionSpec as P

EDGES = 4096
PANEL = 512
BLK = 128
SUB = 8
HI = lax.Precision.HIGHEST
TN = (((0,), (0,)), ((), ()))


def _diag(d_ref):
    wide = 2 * BLK
    lane = lax.broadcasted_iota(jnp.int32, (SUB, wide), 1)
    sub = lax.broadcasted_iota(jnp.int32, (SUB, wide), 0)
    lane_d = lax.broadcasted_iota(jnp.int32, (SUB, BLK), 1)
    sub_d = lax.broadcasted_iota(jnp.int32, (SUB, BLK), 0)
    rows = d_ref[0:SUB, :]
    for p in range(BLK // SUB):
        base = p * SUB
        pick = lane_d == base + sub_d
        for t in range(SUB):
            rowt = jnp.broadcast_to(rows[t:t + 1, :], (SUB, wide))
            head = rowt[:, :BLK]
            c = jnp.sum(jnp.where(pick, head, 0.0), axis=1, keepdims=True)
            piv = jnp.sum(jnp.where(lane_d == base + t, head, 0.0), axis=1, keepdims=True)
            inv = lax.rsqrt(piv)
            u = jnp.where(lane >= base + t, rowt * inv, 0.0)
            rows = jnp.where(sub > t, rows - (c * (inv * inv)) * rowt,
                             jnp.where(sub == t, u, rows))
        d_ref[base:base + SUB, :] = rows
        nb0 = base + SUB
        if nb0 < BLK:
            nxt = d_ref[nb0:nb0 + SUB, :]
            pick2 = lane_d == nb0 + sub_d
            for t in range(SUB):
                rowt = jnp.broadcast_to(rows[t:t + 1, :], (SUB, wide))
                coef = jnp.sum(jnp.where(pick2, rowt[:, :BLK], 0.0), axis=1, keepdims=True)
                nxt = nxt - coef * rowt
            lo = nb0 + SUB
            if lo < BLK:
                upd = lax.dot_general(rows[:, :BLK], rows, TN, precision=HI,
                                      preferred_element_type=jnp.float32)
                d_ref[lo:BLK, :] = d_ref[lo:BLK, :] - upd[lo:, :]
            rows = nxt


def _chol_rows_kernel(a_ref, o_ref, d_ref):
    n, width = a_ref.shape[0], a_ref.shape[1]
    o_ref[...] = a_ref[...]
    nb = n // BLK
    wide = 2 * BLK
    eye = (lax.broadcasted_iota(jnp.int32, (BLK, BLK), 0)
           == lax.broadcasted_iota(jnp.int32, (BLK, BLK), 1)).astype(jnp.float32)
    for k in range(nb):
        r0 = k * BLK
        m = width - r0
        d_ref[:, :BLK] = o_ref[pl.ds(r0, BLK), pl.ds(r0, BLK)]
        d_ref[:, BLK:] = eye

        _diag(d_ref)
        o_ref[pl.ds(r0, BLK), pl.ds(r0, BLK)] = d_ref[:, :BLK]
        if m > BLK:
            rest = o_ref[pl.ds(r0, BLK), pl.ds(r0 + BLK, m - BLK)]
            o_ref[pl.ds(r0, BLK), pl.ds(r0 + BLK, m - BLK)] = jnp.dot(
                d_ref[:, BLK:], rest, precision=HI, preferred_element_type=jnp.float32)
        for j in range(k + 1, nb):
            c0 = j * BLK
            coef = o_ref[pl.ds(r0, BLK), pl.ds(c0, BLK)]
            right = o_ref[pl.ds(r0, BLK), pl.ds(c0, width - c0)]
            upd = lax.dot_general(coef, right, TN, precision=HI,
                                  preferred_element_type=jnp.float32)
            o_ref[pl.ds(c0, BLK), pl.ds(c0, width - c0)] -= upd


def chol_rows(aug, interpret=False):
    return pl.pallas_call(
        _chol_rows_kernel,
        out_shape=jax.ShapeDtypeStruct(aug.shape, jnp.float32),
        scratch_shapes=[pltpu.VMEM((BLK, 2 * BLK), jnp.float32)],
        compiler_params=pltpu.CompilerParams(vmem_limit_bytes=48 * 1024 * 1024),
        interpret=interpret,
    )(aug)


def in_one_piece(arrays, axis, dim, along):
    widths = [a.shape[along] for a in arrays]
    both = jnp.concatenate(arrays, axis=along)
    whole = lax.all_gather(both, axis, axis=dim, tiled=True)
    return tuple(jnp.split(whole, [sum(widths[:k]) for k in range(1, len(widths))], axis=along))


def copy_for_each(x, axis):
    count = lax.axis_size(axis)
    return lax.all_to_all(jnp.broadcast_to(x[None], (count, *x.shape)), axis, 0, 0, tiled=True)


def of_everyone(x, axis):
    return copy_for_each(x, axis).sum(axis=0)


def together(arrays, axis):
    ends = [0]
    for a in arrays:
        ends.append(ends[-1] + a.size)
    subtotal = of_everyone(jnp.concatenate([a.ravel() for a in arrays]), axis)
    return tuple((subtotal[b:e].reshape(a.shape) for a, b, e in zip(arrays, ends, ends[1:])))


def in_one_piece_2(arrays, axis, dim, along):
    both = jnp.concatenate(arrays, axis=along)
    whole, at, gathered = (lax.psum_scatter(both, axis, scatter_dimension=dim, tiled=True), 0, [])
    for a in arrays:
        gathered.append(lax.slice_in_dim(whole, at, at + a.shape[along], axis=along))
        at += a.shape[along]
    return tuple(gathered)


def joined_along(tiles, dim):
    dims = list(tiles.shape[1:])
    dims[dim] *= tiles.shape[0]
    return jnp.moveaxis(tiles, 0, dim).reshape(dims)


def gather_directly(x, axis, dim):
    tiles = copy_for_each(x, axis)
    return joined_along(tiles, dim)


def subject_rows(parts, groups, count):
    width = parts.shape[-1]
    return parts.reshape(groups, count, width).transpose(1, 0, 2).reshape(groups * count, width)


def body(feats, prior_factor, ridge):
    groups = lax.axis_size("row")
    lanes = lax.axis_size("col")
    row_pos = lax.axis_index("row")
    col_pos = lax.axis_index("col")
    rows_here = feats.shape[0]
    cols_here = ridge.shape[0]
    total_cols = cols_here * lanes
    leading = total_cols // groups
    col_feats, col_prior = in_one_piece((feats[:leading], prior_factor[:leading]), "row", 0, 1)
    col_feats = subject_rows(col_feats, groups, leading)
    col_prior = subject_rows(col_prior, groups, leading)
    gram_part = jnp.dot(feats, col_feats.T, preferred_element_type=jnp.float32)
    update_part = jnp.dot(prior_factor, col_prior.T, preferred_element_type=jnp.float32)
    wide_feats = feats.astype(jnp.float32)
    wide_cols = col_feats.astype(jnp.float32)
    col_start = col_pos * cols_here
    ridge_pad = lax.dynamic_update_slice_in_dim(
        jnp.zeros((total_cols,), jnp.float32), ridge, col_start, 0)
    row_sq, col_sq, ridge_all = together(
        (jnp.sum(wide_feats * wide_feats, axis=1), jnp.sum(wide_cols * wide_cols, axis=1),
         ridge_pad), "col"
    )

    def system_of(gram, update, sq, first):
        count, width = gram.shape
        start = col_start if width == cols_here else 0
        col_part = lax.dynamic_slice_in_dim(col_sq, start, width)
        kernel = jnp.exp(-(sq[:, None] + col_part[None, :] - 2.0 * gram) / EDGES)
        subject = (lax.broadcasted_iota(jnp.int32, (count, width), 0) + first) * groups + row_pos
        column = lax.broadcasted_iota(jnp.int32, (count, width), 1) + start
        ridge_part = ridge if width == cols_here else ridge_all
        diag = jnp.where(subject == column, ridge_part[None, :], jnp.zeros_like(kernel))
        return kernel + diag - update

    head_part = jnp.concatenate([gram_part[:leading], update_part[:leading]], axis=0)
    head_tiles = head_part.reshape(2 * leading, lanes, cols_here).transpose(1, 0, 2)
    head_sum = lax.all_to_all(head_tiles, "col", 0, 0, tiled=True).sum(axis=0)
    head_gram, head_update = head_sum[:leading], head_sum[leading:]
    head = system_of(head_gram, head_update, row_sq[:leading], 0)
    by_rows = subject_rows(gather_directly(head, "row", 0), groups, leading)
    square = gather_directly(by_rows, "col", 1)
    gram_part, update_part, square = lax.optimization_barrier((gram_part, update_part, square))
    n = square.shape[0]
    i = lax.broadcasted_iota(jnp.int32, (n, n), 0)
    j = lax.broadcasted_iota(jnp.int32, (n, n), 1)
    flipped = square.T
    same = (i < PANEL) == (j < PANEL)
    sym = jnp.where(same, (square + flipped) * 0.5, jnp.where(i < j, flipped, square))
    eye = (i == j).astype(jnp.float32)
    done = chol_rows(jnp.concatenate([sym, eye], axis=1))
    inv_t = lax.dynamic_slice_in_dim(done[:, n:], col_start, cols_here, 0)

    both = lax.psum(jnp.concatenate([gram_part, update_part], axis=0), "col")
    gram, update = both[:rows_here], both[rows_here:]
    system = system_of(gram, update, row_sq, 0)
    return lax.dot_general(system, inv_t, (((1,), (1,)), ((), ())), precision=HI,
                           preferred_element_type=jnp.float32)


def solution(mesh):
    return jax.shard_map(
        body,
        mesh=mesh,
        in_specs=(P("row", "col"), P("row", "col"), P("col")),
        out_specs=P("row", "col"),
        check_vma=False,
    )
```

```python
import jax
import jax.numpy as jnp
from jax import lax
from jax.experimental import pallas as pl
from jax.experimental.pallas import tpu as pltpu
from jax.sharding import PartitionSpec as P

EDGES = 4096
PANEL = 512
BLK = 128
SUB = 8
HI = lax.Precision.HIGHEST
TN = (((0,), (0,)), ((), ()))


def _diag(d_ref):
    wide = 2 * BLK
    lane = lax.broadcasted_iota(jnp.int32, (SUB, wide), 1)
    sub = lax.broadcasted_iota(jnp.int32, (SUB, wide), 0)
    lane_d = lax.broadcasted_iota(jnp.int32, (SUB, BLK), 1)
    sub_d = lax.broadcasted_iota(jnp.int32, (SUB, BLK), 0)
    rows = d_ref[0:SUB, :]
    for p in range(BLK // SUB):
        base = p * SUB
        pick = lane_d == base + sub_d
        for t in range(SUB):
            rowt = jnp.broadcast_to(rows[t:t + 1, :], (SUB, wide))
            head = rowt[:, :BLK]
            c = jnp.sum(jnp.where(pick, head, 0.0), axis=1, keepdims=True)
            piv = jnp.sum(jnp.where(lane_d == base + t, head, 0.0), axis=1, keepdims=True)
            inv = lax.rsqrt(piv)
            u = jnp.where(lane >= base + t, rowt * inv, 0.0)
            rows = jnp.where(sub > t, rows - (c * (inv * inv)) * rowt,
                             jnp.where(sub == t, u, rows))
        d_ref[base:base + SUB, :] = rows
        nb0 = base + SUB
        if nb0 < BLK:
            nxt = d_ref[nb0:nb0 + SUB, :]
            pick2 = lane_d == nb0 + sub_d
            for t in range(SUB):
                rowt = jnp.broadcast_to(rows[t:t + 1, :], (SUB, wide))
                coef = jnp.sum(jnp.where(pick2, rowt[:, :BLK], 0.0), axis=1, keepdims=True)
                nxt = nxt - coef * rowt
            lo = nb0 + SUB
            if lo < BLK:
                upd = lax.dot_general(rows[:, :BLK], rows, TN, precision=HI,
                                      preferred_element_type=jnp.float32)
                d_ref[lo:BLK, :] = d_ref[lo:BLK, :] - upd[lo:, :]
            rows = nxt


def _chol_rows_kernel(a_ref, o_ref, d_ref):
    n, width = a_ref.shape[0], a_ref.shape[1]
    o_ref[...] = a_ref[...]
    nb = n // BLK
    wide = 2 * BLK
    eye = (lax.broadcasted_iota(jnp.int32, (BLK, BLK), 0)
           == lax.broadcasted_iota(jnp.int32, (BLK, BLK), 1)).astype(jnp.float32)
    for k in range(nb):
        r0 = k * BLK
        m = width - r0
        d_ref[:, :BLK] = o_ref[pl.ds(r0, BLK), pl.ds(r0, BLK)]
        d_ref[:, BLK:] = eye

        _diag(d_ref)
        o_ref[pl.ds(r0, BLK), pl.ds(r0, BLK)] = d_ref[:, :BLK]
        if m > BLK:
            rest = o_ref[pl.ds(r0, BLK), pl.ds(r0 + BLK, m - BLK)]
            o_ref[pl.ds(r0, BLK), pl.ds(r0 + BLK, m - BLK)] = jnp.dot(
                d_ref[:, BLK:], rest, precision=HI, preferred_element_type=jnp.float32)
        for j in range(k + 1, nb):
            c0 = j * BLK
            coef = o_ref[pl.ds(r0, BLK), pl.ds(c0, BLK)]
            right = o_ref[pl.ds(r0, BLK), pl.ds(c0, width - c0)]
            upd = lax.dot_general(coef, right, TN, precision=HI,
                                  preferred_element_type=jnp.float32)
            o_ref[pl.ds(c0, BLK), pl.ds(c0, width - c0)] -= upd


def chol_rows(aug, interpret=False):
    return pl.pallas_call(
        _chol_rows_kernel,
        out_shape=jax.ShapeDtypeStruct(aug.shape, jnp.float32),
        scratch_shapes=[pltpu.VMEM((BLK, 2 * BLK), jnp.float32)],
        compiler_params=pltpu.CompilerParams(vmem_limit_bytes=48 * 1024 * 1024),
        interpret=interpret,
    )(aug)


def in_one_piece(arrays, axis, dim, along):
    widths = [a.shape[along] for a in arrays]
    both = jnp.concatenate(arrays, axis=along)
    whole = lax.all_gather(both, axis, axis=dim, tiled=True)
    return tuple(jnp.split(whole, [sum(widths[:k]) for k in range(1, len(widths))], axis=along))


def copy_for_each(x, axis):
    count = lax.axis_size(axis)
    return lax.all_to_all(jnp.broadcast_to(x[None], (count, *x.shape)), axis, 0, 0, tiled=True)


def of_everyone(x, axis):
    return copy_for_each(x, axis).sum(axis=0)


def together(arrays, axis):
    ends = [0]
    for a in arrays:
        ends.append(ends[-1] + a.size)
    subtotal = of_everyone(jnp.concatenate([a.ravel() for a in arrays]), axis)
    return tuple((subtotal[b:e].reshape(a.shape) for a, b, e in zip(arrays, ends, ends[1:])))


def in_one_piece_2(arrays, axis, dim, along):
    both = jnp.concatenate(arrays, axis=along)
    whole, at, gathered = (lax.psum_scatter(both, axis, scatter_dimension=dim, tiled=True), 0, [])
    for a in arrays:
        gathered.append(lax.slice_in_dim(whole, at, at + a.shape[along], axis=along))
        at += a.shape[along]
    return tuple(gathered)


def joined_along(tiles, dim):
    dims = list(tiles.shape[1:])
    dims[dim] *= tiles.shape[0]
    return jnp.moveaxis(tiles, 0, dim).reshape(dims)


def gather_directly(x, axis, dim):
    tiles = copy_for_each(x, axis)
    return joined_along(tiles, dim)


def subject_rows(parts, groups, count):
    width = parts.shape[-1]
    return parts.reshape(groups, count, width).transpose(1, 0, 2).reshape(groups * count, width)


def body(feats, prior_factor, ridge):
    groups = lax.axis_size("row")
    lanes = lax.axis_size("col")
    row_pos = lax.axis_index("row")
    col_pos = lax.axis_index("col")
    rows_here = feats.shape[0]
    cols_here = ridge.shape[0]
    total_cols = cols_here * lanes
    leading = total_cols // groups
    both_cols = gather_directly(jnp.concatenate([feats[:leading], prior_factor[:leading]], axis=1), "row", 0)
    col_feats, col_prior = both_cols[:, :feats.shape[1]], both_cols[:, feats.shape[1]:]
    col_feats = subject_rows(col_feats, groups, leading)
    col_prior = subject_rows(col_prior, groups, leading)
    gram_part = jnp.dot(feats, col_feats.T, preferred_element_type=jnp.float32)
    update_part = jnp.dot(prior_factor, col_prior.T, preferred_element_type=jnp.float32)
    wide_feats = feats.astype(jnp.float32)
    wide_cols = col_feats.astype(jnp.float32)
    col_start = col_pos * cols_here
    ridge_pad = lax.dynamic_update_slice_in_dim(
        jnp.zeros((total_cols,), jnp.float32), ridge, col_start, 0)
    sums = jnp.concatenate([jnp.sum(wide_feats * wide_feats, axis=1),
                            jnp.sum(wide_cols * wide_cols, axis=1), ridge_pad])
    head_part = jnp.concatenate([gram_part[:leading], update_part[:leading]], axis=0)
    head_tiles = head_part.reshape(2 * leading, lanes, cols_here).transpose(1, 0, 2)
    payload = jnp.concatenate(
        [head_tiles.reshape(lanes, -1), jnp.broadcast_to(sums[None], (lanes, sums.shape[0]))], axis=1)
    got = lax.all_to_all(payload, "col", 0, 0, tiled=True).sum(axis=0)
    tile_size = 2 * leading * cols_here
    head_sum = got[:tile_size].reshape(2 * leading, cols_here)
    row_sq = got[tile_size:tile_size + rows_here]
    col_sq = got[tile_size + rows_here:tile_size + rows_here + total_cols]
    ridge_all = got[tile_size + rows_here + total_cols:]

    def system_of(gram, update, sq, first):
        count, width = gram.shape
        start = col_start if width == cols_here else 0
        col_part = lax.dynamic_slice_in_dim(col_sq, start, width)
        kernel = jnp.exp(-(sq[:, None] + col_part[None, :] - 2.0 * gram) / EDGES)
        subject = (lax.broadcasted_iota(jnp.int32, (count, width), 0) + first) * groups + row_pos
        column = lax.broadcasted_iota(jnp.int32, (count, width), 1) + start
        ridge_part = ridge if width == cols_here else ridge_all
        diag = jnp.where(subject == column, ridge_part[None, :], jnp.zeros_like(kernel))
        return kernel + diag - update

    head_gram, head_update = head_sum[:leading], head_sum[leading:]
    head = system_of(head_gram, head_update, row_sq[:leading], 0)
    by_rows = subject_rows(gather_directly(head, "row", 0), groups, leading)
    square = gather_directly(by_rows, "col", 1)
    gram_part, update_part, square = lax.optimization_barrier((gram_part, update_part, square))
    n = square.shape[0]
    i = lax.broadcasted_iota(jnp.int32, (n, n), 0)
    j = lax.broadcasted_iota(jnp.int32, (n, n), 1)
    flipped = square.T
    same = (i < PANEL) == (j < PANEL)
    sym = jnp.where(same, (square + flipped) * 0.5, jnp.where(i < j, flipped, square))
    eye = (i == j).astype(jnp.float32)
    done = chol_rows(jnp.concatenate([sym, eye], axis=1))
    inv_t = lax.dynamic_slice_in_dim(done[:, n:], col_start, cols_here, 0)

    both = lax.psum(jnp.concatenate([gram_part, update_part], axis=0), "col")
    gram, update = both[:rows_here], both[rows_here:]
    system = system_of(gram, update, row_sq, 0)
    return lax.dot_general(system, inv_t, (((1,), (1,)), ((), ())), precision=HI,
                           preferred_element_type=jnp.float32)


def solution(mesh):
    return jax.shard_map(
        body,
        mesh=mesh,
        in_specs=(P("row", "col"), P("row", "col"), P("col")),
        out_specs=P("row", "col"),
        check_vma=False,
    )
```

```python
import jax
import jax.numpy as jnp
from jax import lax
from jax.experimental import pallas as pl
from jax.experimental.pallas import tpu as pltpu
from jax.sharding import PartitionSpec as P

EDGES = 4096
PANEL = 512
BLK = 128
SUB = 8
HI = lax.Precision.HIGHEST
TN = (((0,), (0,)), ((), ()))


def _diag(d_ref):
    wide = 2 * BLK
    lane = lax.broadcasted_iota(jnp.int32, (SUB, wide), 1)
    sub = lax.broadcasted_iota(jnp.int32, (SUB, wide), 0)
    lane_d = lax.broadcasted_iota(jnp.int32, (SUB, BLK), 1)
    sub_d = lax.broadcasted_iota(jnp.int32, (SUB, BLK), 0)
    rows = d_ref[0:SUB, :]
    for p in range(BLK // SUB):
        base = p * SUB
        pick = lane_d == base + sub_d
        for t in range(SUB):
            rowt = jnp.broadcast_to(rows[t:t + 1, :], (SUB, wide))
            head = rowt[:, :BLK]
            c = jnp.sum(jnp.where(pick, head, 0.0), axis=1, keepdims=True)
            piv = jnp.sum(jnp.where(lane_d == base + t, head, 0.0), axis=1, keepdims=True)
            inv = lax.rsqrt(piv)
            u = jnp.where(lane >= base + t, rowt * inv, 0.0)
            rows = jnp.where(sub > t, rows - (c * (inv * inv)) * rowt,
                             jnp.where(sub == t, u, rows))
        d_ref[base:base + SUB, :] = rows
        nb0 = base + SUB
        if nb0 < BLK:
            nxt = d_ref[nb0:nb0 + SUB, :]
            pick2 = lane_d == nb0 + sub_d
            for t in range(SUB):
                rowt = jnp.broadcast_to(rows[t:t + 1, :], (SUB, wide))
                coef = jnp.sum(jnp.where(pick2, rowt[:, :BLK], 0.0), axis=1, keepdims=True)
                nxt = nxt - coef * rowt
            lo = nb0 + SUB
            if lo < BLK:
                upd = lax.dot_general(rows[:, :BLK], rows, TN, precision=HI,
                                      preferred_element_type=jnp.float32)
                d_ref[lo:BLK, :] = d_ref[lo:BLK, :] - upd[lo:, :]
            rows = nxt


def _chol_rows_kernel(a_ref, o_ref, d_ref):
    n, width = a_ref.shape[0], a_ref.shape[1]
    o_ref[...] = a_ref[...]
    nb = n // BLK
    wide = 2 * BLK
    eye = (lax.broadcasted_iota(jnp.int32, (BLK, BLK), 0)
           == lax.broadcasted_iota(jnp.int32, (BLK, BLK), 1)).astype(jnp.float32)
    for k in range(nb):
        r0 = k * BLK
        m = width - r0
        d_ref[:, :BLK] = o_ref[pl.ds(r0, BLK), pl.ds(r0, BLK)]
        d_ref[:, BLK:] = eye

        _diag(d_ref)
        o_ref[pl.ds(r0, BLK), pl.ds(r0, BLK)] = d_ref[:, :BLK]
        if m > BLK:
            rest = o_ref[pl.ds(r0, BLK), pl.ds(r0 + BLK, m - BLK)]
            o_ref[pl.ds(r0, BLK), pl.ds(r0 + BLK, m - BLK)] = jnp.dot(
                d_ref[:, BLK:], rest, precision=HI, preferred_element_type=jnp.float32)
        for j in range(k + 1, nb):
            c0 = j * BLK
            coef = o_ref[pl.ds(r0, BLK), pl.ds(c0, BLK)]
            right = o_ref[pl.ds(r0, BLK), pl.ds(c0, width - c0)]
            upd = lax.dot_general(coef, right, TN, precision=HI,
                                  preferred_element_type=jnp.float32)
            o_ref[pl.ds(c0, BLK), pl.ds(c0, width - c0)] -= upd


def chol_rows(aug, interpret=False):
    return pl.pallas_call(
        _chol_rows_kernel,
        out_shape=jax.ShapeDtypeStruct(aug.shape, jnp.float32),
        scratch_shapes=[pltpu.VMEM((BLK, 2 * BLK), jnp.float32)],
        compiler_params=pltpu.CompilerParams(vmem_limit_bytes=48 * 1024 * 1024),
        interpret=interpret,
    )(aug)


def in_one_piece(arrays, axis, dim, along):
    widths = [a.shape[along] for a in arrays]
    both = jnp.concatenate(arrays, axis=along)
    whole = lax.all_gather(both, axis, axis=dim, tiled=True)
    return tuple(jnp.split(whole, [sum(widths[:k]) for k in range(1, len(widths))], axis=along))


def copy_for_each(x, axis):
    count = lax.axis_size(axis)
    return lax.all_to_all(jnp.broadcast_to(x[None], (count, *x.shape)), axis, 0, 0, tiled=True)


def of_everyone(x, axis):
    return copy_for_each(x, axis).sum(axis=0)


def together(arrays, axis):
    ends = [0]
    for a in arrays:
        ends.append(ends[-1] + a.size)
    subtotal = of_everyone(jnp.concatenate([a.ravel() for a in arrays]), axis)
    return tuple((subtotal[b:e].reshape(a.shape) for a, b, e in zip(arrays, ends, ends[1:])))


def in_one_piece_2(arrays, axis, dim, along):
    both = jnp.concatenate(arrays, axis=along)
    whole, at, gathered = (lax.psum_scatter(both, axis, scatter_dimension=dim, tiled=True), 0, [])
    for a in arrays:
        gathered.append(lax.slice_in_dim(whole, at, at + a.shape[along], axis=along))
        at += a.shape[along]
    return tuple(gathered)


def joined_along(tiles, dim):
    dims = list(tiles.shape[1:])
    dims[dim] *= tiles.shape[0]
    return jnp.moveaxis(tiles, 0, dim).reshape(dims)


def gather_directly(x, axis, dim):
    tiles = copy_for_each(x, axis)
    return joined_along(tiles, dim)


def subject_rows(parts, groups, count):
    width = parts.shape[-1]
    return parts.reshape(groups, count, width).transpose(1, 0, 2).reshape(groups * count, width)


def body(feats, prior_factor, ridge):
    groups = lax.axis_size("row")
    lanes = lax.axis_size("col")
    row_pos = lax.axis_index("row")
    col_pos = lax.axis_index("col")
    rows_here = feats.shape[0]
    cols_here = ridge.shape[0]
    total_cols = cols_here * lanes
    leading = total_cols // groups
    col_feats, col_prior = in_one_piece((feats[:leading], prior_factor[:leading]), "row", 0, 1)
    col_feats = subject_rows(col_feats, groups, leading)
    col_prior = subject_rows(col_prior, groups, leading)
    gram_part = jnp.dot(feats, col_feats.T, preferred_element_type=jnp.float32)
    update_part = jnp.dot(prior_factor, col_prior.T, preferred_element_type=jnp.float32)
    wide_feats = feats.astype(jnp.float32)
    wide_cols = col_feats.astype(jnp.float32)
    col_start = col_pos * cols_here
    ridge_pad = lax.dynamic_update_slice_in_dim(
        jnp.zeros((total_cols,), jnp.float32), ridge, col_start, 0)
    sums = jnp.concatenate([jnp.sum(wide_feats * wide_feats, axis=1),
                            jnp.sum(wide_cols * wide_cols, axis=1), ridge_pad])
    head_part = jnp.concatenate([gram_part[:leading], update_part[:leading]], axis=0)
    head_tiles = head_part.reshape(2 * leading, lanes, cols_here).transpose(1, 0, 2)
    payload = jnp.concatenate(
        [head_tiles.reshape(lanes, -1), jnp.broadcast_to(sums[None], (lanes, sums.shape[0]))], axis=1)
    got = lax.all_to_all(payload, "col", 0, 0, tiled=True).sum(axis=0)
    tile_size = 2 * leading * cols_here
    head_sum = got[:tile_size].reshape(2 * leading, cols_here)
    row_sq = got[tile_size:tile_size + rows_here]
    col_sq = got[tile_size + rows_here:tile_size + rows_here + total_cols]
    ridge_all = got[tile_size + rows_here + total_cols:]

    def system_of(gram, update, sq, first):
        count, width = gram.shape
        start = col_start if width == cols_here else 0
        col_part = lax.dynamic_slice_in_dim(col_sq, start, width)
        kernel = jnp.exp(-(sq[:, None] + col_part[None, :] - 2.0 * gram) / EDGES)
        subject = (lax.broadcasted_iota(jnp.int32, (count, width), 0) + first) * groups + row_pos
        column = lax.broadcasted_iota(jnp.int32, (count, width), 1) + start
        ridge_part = ridge if width == cols_here else ridge_all
        diag = jnp.where(subject == column, ridge_part[None, :], jnp.zeros_like(kernel))
        return kernel + diag - update

    head_gram, head_update = head_sum[:leading], head_sum[leading:]
    head = system_of(head_gram, head_update, row_sq[:leading], 0)
    by_rows = subject_rows(gather_directly(head, "row", 0), groups, leading)
    square = gather_directly(by_rows, "col", 1)
    gram_part, update_part, square = lax.optimization_barrier((gram_part, update_part, square))
    n = square.shape[0]
    i = lax.broadcasted_iota(jnp.int32, (n, n), 0)
    j = lax.broadcasted_iota(jnp.int32, (n, n), 1)
    flipped = square.T
    same = (i < PANEL) == (j < PANEL)
    sym = jnp.where(same, (square + flipped) * 0.5, jnp.where(i < j, flipped, square))
    eye = (i == j).astype(jnp.float32)
    done = chol_rows(jnp.concatenate([sym, eye], axis=1))
    inv_t = lax.dynamic_slice_in_dim(done[:, n:], col_start, cols_here, 0)

    both = lax.psum(jnp.concatenate([gram_part, update_part], axis=0), "col")
    gram, update = both[:rows_here], both[rows_here:]
    system = system_of(gram, update, row_sq, 0)
    return lax.dot_general(system, inv_t, (((1,), (1,)), ((), ())), precision=HI,
                           preferred_element_type=jnp.float32)


def solution(mesh):
    return jax.shard_map(
        body,
        mesh=mesh,
        in_specs=(P("row", "col"), P("row", "col"), P("col")),
        out_specs=P("row", "col"),
        check_vma=False,
    )
```

```python
import jax
import jax.numpy as jnp
from jax import lax
from jax.experimental import pallas as pl
from jax.experimental.pallas import tpu as pltpu
from jax.sharding import PartitionSpec as P

EDGES = 4096
PANEL = 512
BLK = 128
SUB = 8
HI = lax.Precision.HIGHEST
TN = (((0,), (0,)), ((), ()))


def _diag(d_ref):
    wide = 2 * BLK
    lane = lax.broadcasted_iota(jnp.int32, (SUB, wide), 1)
    sub = lax.broadcasted_iota(jnp.int32, (SUB, wide), 0)
    lane_d = lax.broadcasted_iota(jnp.int32, (SUB, BLK), 1)
    sub_d = lax.broadcasted_iota(jnp.int32, (SUB, BLK), 0)
    rows = d_ref[0:SUB, :]
    for p in range(BLK // SUB):
        base = p * SUB
        pick = lane_d == base + sub_d
        for t in range(SUB):
            rowt = jnp.broadcast_to(rows[t:t + 1, :], (SUB, wide))
            head = rowt[:, :BLK]
            c = jnp.sum(jnp.where(pick, head, 0.0), axis=1, keepdims=True)
            piv = jnp.sum(jnp.where(lane_d == base + t, head, 0.0), axis=1, keepdims=True)
            inv = lax.rsqrt(piv)
            u = jnp.where(lane >= base + t, rowt * inv, 0.0)
            rows = jnp.where(sub > t, rows - (c * (inv * inv)) * rowt,
                             jnp.where(sub == t, u, rows))
        d_ref[base:base + SUB, :] = rows
        nb0 = base + SUB
        if nb0 < BLK:
            nxt = d_ref[nb0:nb0 + SUB, :]
            pick2 = lane_d == nb0 + sub_d
            for t in range(SUB):
                rowt = jnp.broadcast_to(rows[t:t + 1, :], (SUB, wide))
                coef = jnp.sum(jnp.where(pick2, rowt[:, :BLK], 0.0), axis=1, keepdims=True)
                nxt = nxt - coef * rowt
            lo = nb0 + SUB
            if lo < BLK:
                upd = lax.dot_general(rows[:, :BLK], rows, TN, precision=HI,
                                      preferred_element_type=jnp.float32)
                d_ref[lo:BLK, :] = d_ref[lo:BLK, :] - upd[lo:, :]
            rows = nxt


def _chol_rows_kernel(a_ref, o_ref, d_ref):
    n, width = a_ref.shape[0], a_ref.shape[1]
    o_ref[...] = a_ref[...]
    nb = n // BLK
    wide = 2 * BLK
    eye = (lax.broadcasted_iota(jnp.int32, (BLK, BLK), 0)
           == lax.broadcasted_iota(jnp.int32, (BLK, BLK), 1)).astype(jnp.float32)
    for k in range(nb):
        r0 = k * BLK
        m = width - r0
        d_ref[:, :BLK] = o_ref[pl.ds(r0, BLK), pl.ds(r0, BLK)]
        d_ref[:, BLK:] = eye

        _diag(d_ref)
        o_ref[pl.ds(r0, BLK), pl.ds(r0, BLK)] = d_ref[:, :BLK]
        if m > BLK:
            rest = o_ref[pl.ds(r0, BLK), pl.ds(r0 + BLK, m - BLK)]
            o_ref[pl.ds(r0, BLK), pl.ds(r0 + BLK, m - BLK)] = jnp.dot(
                d_ref[:, BLK:], rest, precision=HI, preferred_element_type=jnp.float32)
        for j in range(k + 1, nb):
            c0 = j * BLK
            coef = o_ref[pl.ds(r0, BLK), pl.ds(c0, BLK)]
            right = o_ref[pl.ds(r0, BLK), pl.ds(c0, width - c0)]
            upd = lax.dot_general(coef, right, TN, precision=HI,
                                  preferred_element_type=jnp.float32)
            o_ref[pl.ds(c0, BLK), pl.ds(c0, width - c0)] -= upd


def chol_rows(aug, interpret=False):
    return pl.pallas_call(
        _chol_rows_kernel,
        out_shape=jax.ShapeDtypeStruct(aug.shape, jnp.float32),
        scratch_shapes=[pltpu.VMEM((BLK, 2 * BLK), jnp.float32)],
        compiler_params=pltpu.CompilerParams(vmem_limit_bytes=48 * 1024 * 1024),
        interpret=interpret,
    )(aug)


def in_one_piece(arrays, axis, dim, along):
    widths = [a.shape[along] for a in arrays]
    both = jnp.concatenate(arrays, axis=along)
    whole = lax.all_gather(both, axis, axis=dim, tiled=True)
    return tuple(jnp.split(whole, [sum(widths[:k]) for k in range(1, len(widths))], axis=along))


def copy_for_each(x, axis):
    count = lax.axis_size(axis)
    return lax.all_to_all(jnp.broadcast_to(x[None], (count, *x.shape)), axis, 0, 0, tiled=True)


def of_everyone(x, axis):
    return copy_for_each(x, axis).sum(axis=0)


def together(arrays, axis):
    ends = [0]
    for a in arrays:
        ends.append(ends[-1] + a.size)
    subtotal = of_everyone(jnp.concatenate([a.ravel() for a in arrays]), axis)
    return tuple((subtotal[b:e].reshape(a.shape) for a, b, e in zip(arrays, ends, ends[1:])))


def in_one_piece_2(arrays, axis, dim, along):
    both = jnp.concatenate(arrays, axis=along)
    whole, at, gathered = (lax.psum_scatter(both, axis, scatter_dimension=dim, tiled=True), 0, [])
    for a in arrays:
        gathered.append(lax.slice_in_dim(whole, at, at + a.shape[along], axis=along))
        at += a.shape[along]
    return tuple(gathered)


def joined_along(tiles, dim):
    dims = list(tiles.shape[1:])
    dims[dim] *= tiles.shape[0]
    return jnp.moveaxis(tiles, 0, dim).reshape(dims)


def gather_directly(x, axis, dim):
    tiles = copy_for_each(x, axis)
    return joined_along(tiles, dim)


def subject_rows(parts, groups, count):
    width = parts.shape[-1]
    return parts.reshape(groups, count, width).transpose(1, 0, 2).reshape(groups * count, width)


def body(feats, prior_factor, ridge):
    groups = lax.axis_size("row")
    lanes = lax.axis_size("col")
    row_pos = lax.axis_index("row")
    col_pos = lax.axis_index("col")
    rows_here = feats.shape[0]
    cols_here = ridge.shape[0]
    total_cols = cols_here * lanes
    leading = total_cols // groups
    col_feats, col_prior = in_one_piece((feats[:leading], prior_factor[:leading]), "row", 0, 1)
    col_feats = subject_rows(col_feats, groups, leading)
    col_prior = subject_rows(col_prior, groups, leading)
    gram_part = jnp.dot(feats, col_feats.T, preferred_element_type=jnp.float32)
    update_part = jnp.dot(prior_factor, col_prior.T, preferred_element_type=jnp.float32)
    wide_feats = feats.astype(jnp.float32)
    wide_cols = col_feats.astype(jnp.float32)
    col_start = col_pos * cols_here
    ridge_pad = lax.dynamic_update_slice_in_dim(
        jnp.zeros((total_cols,), jnp.float32), ridge, col_start, 0)
    row_sq, col_sq, ridge_all = together(
        (jnp.sum(wide_feats * wide_feats, axis=1), jnp.sum(wide_cols * wide_cols, axis=1),
         ridge_pad), "col"
    )

    def system_of(gram, update, sq, first):
        count, width = gram.shape
        start = col_start if width == cols_here else 0
        col_part = lax.dynamic_slice_in_dim(col_sq, start, width)
        kernel = jnp.exp(-(sq[:, None] + col_part[None, :] - 2.0 * gram) / EDGES)
        subject = (lax.broadcasted_iota(jnp.int32, (count, width), 0) + first) * groups + row_pos
        column = lax.broadcasted_iota(jnp.int32, (count, width), 1) + start
        ridge_part = ridge if width == cols_here else ridge_all
        diag = jnp.where(subject == column, ridge_part[None, :], jnp.zeros_like(kernel))
        return kernel + diag - update

    head_part = jnp.concatenate([gram_part[:leading], update_part[:leading]], axis=0)
    head_tiles = head_part.reshape(2 * leading, lanes, cols_here).transpose(1, 0, 2)
    head_sum = lax.all_to_all(head_tiles, "col", 0, 0, tiled=True).sum(axis=0)
    head_gram, head_update = head_sum[:leading], head_sum[leading:]
    head = system_of(head_gram, head_update, row_sq[:leading], 0)
    by_rows = subject_rows(gather_directly(head, "row", 0), groups, leading)
    square = gather_directly(by_rows, "col", 1)
    gram_part, update_part, square = lax.optimization_barrier((gram_part, update_part, square))
    n = square.shape[0]
    i = lax.broadcasted_iota(jnp.int32, (n, n), 0)
    j = lax.broadcasted_iota(jnp.int32, (n, n), 1)
    flipped = square.T
    same = (i < PANEL) == (j < PANEL)
    sym = jnp.where(same, (square + flipped) * 0.5, jnp.where(i < j, flipped, square))
    eye = (i == j).astype(jnp.float32)
    done = chol_rows(jnp.concatenate([sym, eye], axis=1))
    inv_t = lax.dynamic_slice(done, (col_start, n), (cols_here, n))

    both = lax.psum(jnp.concatenate([gram_part, update_part], axis=0), "col")
    gram, update = both[:rows_here], both[rows_here:]
    system = system_of(gram, update, row_sq, 0)
    return lax.dot_general(system, inv_t, (((1,), (1,)), ((), ())), precision=HI,
                           preferred_element_type=jnp.float32)


def solution(mesh):
    return jax.shard_map(
        body,
        mesh=mesh,
        in_specs=(P("row", "col"), P("row", "col"), P("col")),
        out_specs=P("row", "col"),
        check_vma=False,
    )
```
